768 devices in a mesh: lat: 192 (over y_lo, x, z, core), lon: 4 (over y_hi).
Axes of the slice: x: 4, y: 8 (y_hi: 4, y_lo: 2; y = y_hi * 2 + y_lo), z: 12, core: 2. Of those that a mesh axis runs over, the one named last changes fastest.
Arguments:
- fields: bfloat16 [2, 192, 2048, 256], P(None, 'lat', 'lon'), may hold values from -6 to 6
- norm_gain: float32 [256], replicated, may hold values from 0.1 to 1.9
- w_qkv: bfloat16 [256, 768], replicated, may hold values from -12 to 12
- w_out: bfloat16 [256, 256], replicated, may hold values from -1 to 1
- conv_weight: bfloat16 [256, 4, 4, 128], replicated, may hold values from -0.1875 to 0.1875
- conv_bias: float32 [128], replicated, may hold values from -3 to 3
Outputs:
- upsampled: bfloat16 [2, 384, 4096, 128], P(None, 'lat', 'lon')
The draws below stay inside these ranges and needn't reach their ends.
All inputs are finite; a program needn't handle non-finite values.
Results may differ from the reference program's by a relative error of at most 0.0085.
Values may be sent and summed in bfloat16 or wider, within the bound.
No kernel may reach another device: no remote copies, remote signals or barrier semaphores. Data moves between devices by JAX's collectives and lax.ppermute only.
A program may use at most 64 MiB of HBM per device.

```python
import math
import jax
import jax.numpy as jnp
from jax import lax

C = 256
HEADS = 8
CO = 128
B = 2
LAT = 192
LON = 2048


def common_pattern(key):
    pattern_key = jax.random.fold_in(key, 7)
    halves = (jax.random.randint(pattern_key, (C // 2,), 0, 2) * 2 - 1).astype(jnp.float32)
    paired = jnp.stack([halves, -halves], axis=1).reshape(C)
    return paired * C ** (-0.5)


def column_signs(key):
    sign_key = jax.random.fold_in(key, 13)
    return (jax.random.randint(sign_key, (C,), 0, 2) * 2 - 1).astype(jnp.float32)


def draw_fields(key, part):
    pattern = common_pattern(key)
    noise_key, column_key = jax.random.split(jax.random.fold_in(key, 11), 2)
    column = jax.random.randint(column_key, (B, LAT), 0, LON)
    noise = jnp.clip(jax.random.normal(noise_key, (B, LAT, LON, C), jnp.float32), -6.0, 6.0)
    share = 0.5
    marked = (jnp.arange(LON)[None, None, :] == column[..., None]).astype(jnp.float32)[..., None]
    scale = C ** 0.5
    drawn = share * scale * pattern + (1.0 - share * share) ** 0.5 * noise
    landmark = 0.95 * scale * pattern + 0.31 * noise
    result = marked * landmark + (1.0 - marked) * drawn
    return result.astype(jnp.bfloat16)


def draw_w_qkv(key, part):
    first_key = jax.random.fold_in(key, 0)
    factor = C ** (-0.5)
    base = jnp.clip(jax.random.normal(first_key, (C, 3 * C), jnp.float32), -6.0, 6.0) * factor
    pattern = common_pattern(key)
    step_scale = math.log(LON) / (C * 0.5 * 0.45)
    magnitude = (step_scale / (C // HEADS) ** 0.5) ** 0.5
    shared = pattern[:, None] * (magnitude * column_signs(key))[None, :]
    query_block = 0.3 * base[:, :C] + shared
    key_block = 0.3 * base[:, C:2 * C] + shared
    result = jnp.concatenate([query_block, key_block, base[:, 2 * C:]], axis=1)
    return result.astype(jnp.bfloat16)


def gaussian(rng, extent, spread, bound, dtype=jnp.bfloat16):
    return jnp.clip(spread * jax.random.normal(rng, extent, jnp.float32), -bound, bound).astype(dtype)


def setup_inputs(seed: int = 0) -> dict:
    seeds = jax.random.split(jax.random.key(seed), 7)
    return {
        "fields": draw_fields(jax.random.fold_in(seeds[6], 71), 0),
        "norm_gain": jnp.clip(1.0 + 0.18 * jax.random.normal(seeds[1], (C,), jnp.float32), 0.1, 1.9),
        "w_qkv": draw_w_qkv(jax.random.fold_in(seeds[6], 71), 0),
        "w_out": gaussian(seeds[3], (C, C), (C // 8) ** -0.5, 1.0),
        "conv_weight": gaussian(seeds[4], (C, 4, 4, CO), (4 * C) ** -0.5, 0.1875),
        "conv_bias": gaussian(seeds[5], (CO,), 0.5, 3.0, jnp.float32),
    }


def normalize(fields, norm_gain):
    values = fields.astype(jnp.float32)
    average = lax.optimization_barrier(jnp.mean(values, axis=-1, keepdims=True))
    centred = values - average
    variance = lax.optimization_barrier(jnp.mean(centred * centred, axis=-1, keepdims=True))
    return (centred * lax.rsqrt(variance + 1e-05) * norm_gain).astype(jnp.bfloat16)

def split_heads(row_block, head_count):
    seq_count, length, width = row_block.shape
    depth = width // head_count
    return row_block.reshape(seq_count, length, head_count, depth).transpose(0, 2, 1, 3).reshape(seq_count * head_count, length, depth)

def merge_heads(row_block, head_count):
    total_items, length, depth = row_block.shape
    seq_count = total_items // head_count
    return row_block.reshape(seq_count, head_count, length, depth).transpose(0, 2, 1, 3).reshape(seq_count, length, head_count * depth)

def attend_one(item_rows):
    query_one, key_one, value_one = item_rows
    scores = jnp.dot(query_one, key_one.T, preferred_element_type=jnp.float32) * query_one.shape[-1] ** (-0.5)
    maxima = lax.optimization_barrier(jnp.max(scores, axis=-1, keepdims=True))
    probs = jnp.exp(scores - maxima)
    totals = lax.optimization_barrier(jnp.sum(probs, axis=-1, keepdims=True))
    summed = jnp.dot(probs.astype(jnp.bfloat16), value_one, preferred_element_type=jnp.float32)
    return summed / totals

def attend_full(queries, keys_rows, values_rows, head_count):
    result = lax.map(attend_one, (split_heads(queries, head_count), split_heads(keys_rows, head_count), split_heads(values_rows, head_count)))
    return merge_heads(result, head_count).astype(jnp.bfloat16)

def upsample(sample, conv_weight, conv_bias):
    width = sample.shape[-1]
    outward = conv_weight.shape[-1]
    accum = jnp.zeros((LAT + 1, 2, LON + 1, 2, outward), jnp.float32)
    flat_rows = sample.reshape(-1, width)
    for row_tap in range(4):
        for col_tap in range(4):
            term = jnp.dot(flat_rows, conv_weight[:, row_tap, col_tap, :], preferred_element_type=jnp.float32).reshape(LAT, LON, outward)
            row_off = row_tap // 2
            col_off = col_tap // 2
            accum = accum.at[row_off:row_off + LAT, row_tap % 2, col_off:col_off + LON, col_tap % 2].add(term)
    tiled = accum.reshape(2 * LAT + 2, 2 * LON + 2, outward)
    middle = tiled[1:-1, 1:-1]
    middle = middle.at[:, 0].add(tiled[1:-1, -1]).at[:, -1].add(tiled[1:-1, 0])
    return (middle + conv_bias).astype(jnp.bfloat16)

def reference(fields, norm_gain, w_qkv, w_out, conv_weight, conv_bias):
    width = fields.shape[-1]
    normed = normalize(fields, norm_gain)
    flat_rows = normed.reshape(-1, width)
    projected = jnp.dot(flat_rows, w_qkv, preferred_element_type=jnp.float32).astype(jnp.bfloat16)
    projected = projected.reshape(B * LAT, LON, 3 * width)
    attended = attend_full(projected[..., :width], projected[..., width:2 * width], projected[..., 2 * width:], HEADS)
    update = jnp.dot(attended.reshape(-1, width), w_out, preferred_element_type=jnp.float32).reshape(fields.shape)
    hidden = (fields.astype(jnp.float32) + update).astype(jnp.bfloat16)
    return lax.map(lambda sample: upsample(sample, conv_weight, conv_bias), hidden)
```

```python
import jax
import jax.numpy as jnp
from jax import lax
from jax.experimental import pallas as pl
from jax.experimental.pallas import tpu as pltpu
from jax.sharding import PartitionSpec as P

HEADS = 8


def extended(block, sides, width, periodic):
    for axis, dim in sides:
        count = lax.axis_size(axis)
        forward = [(i, i + 1) for i in range(count - 1)]
        if periodic:
            forward.append((count - 1, 0))
        backward = [(target, source) for source, target in forward]
        low = lax.ppermute(
            lax.slice_in_dim(block, block.shape[dim] - width, None, axis=dim), axis, forward
        )
        high = lax.ppermute(lax.slice_in_dim(block, 0, width, axis=dim), axis, backward)
        block = jnp.concatenate([low, block, high], axis=dim)
    return block


def normalize(fields, norm_gain):
    values = fields.astype(jnp.float32)
    average = jnp.mean(values, axis=-1, keepdims=True)
    centred = values - average
    variance = jnp.mean(centred * centred, axis=-1, keepdims=True)
    return (centred * lax.rsqrt(variance + 1e-05) * norm_gain).astype(jnp.bfloat16)


def attn_kernel(q_ref, kt_ref, v_ref, o_ref):
    q = q_ref[0]
    kt = kt_ref[0]
    v = v_ref[0]
    scale = q.shape[-1] ** (-0.5)
    s = jnp.dot(q, kt, preferred_element_type=jnp.float32) * scale
    m = jnp.max(s, axis=-1, keepdims=True)
    p = jnp.exp(s - m)
    l = jnp.sum(p, axis=-1, keepdims=True)
    o = jnp.dot(p.astype(jnp.bfloat16), v, preferred_element_type=jnp.float32)
    o_ref[0] = (o / l).astype(o_ref.dtype)


def attention(qh, kt, vh, tq):
    items, lq, depth = qh.shape
    lk = kt.shape[-1]
    return pl.pallas_call(
        attn_kernel,
        grid=(items, lq // tq),
        in_specs=[
            pl.BlockSpec((1, tq, depth), lambda i, j: (i, j, 0)),
            pl.BlockSpec((1, depth, lk), lambda i, j: (i, 0, 0)),
            pl.BlockSpec((1, lk, depth), lambda i, j: (i, 0, 0)),
        ],
        out_specs=pl.BlockSpec((1, tq, depth), lambda i, j: (i, j, 0)),
        out_shape=jax.ShapeDtypeStruct((items, lq, depth), jnp.bfloat16),
        compiler_params=pltpu.CompilerParams(vmem_limit_bytes=48 * 1024 * 1024),
    )(qh, kt, vh)


def tap_tile(hidden, conv_weight):
    batch_size, row_count, col_count, width = hidden.shape
    outward = conv_weight.shape[-1]
    taps = jnp.dot(
        hidden.reshape(-1, width),
        conv_weight.reshape(width, 16 * outward),
        preferred_element_type=jnp.float32,
    )
    taps = taps.reshape(batch_size, row_count, col_count, 2, 2, 2, 2, outward)
    total_tile = jnp.zeros((batch_size, row_count + 1, 2, col_count + 1, 2, outward), jnp.float32)
    for row_half in range(2):
        for col_half in range(2):
            portion = taps[:, :, :, row_half, :, col_half, :, :].transpose(0, 1, 3, 2, 4, 5)
            portion = jnp.pad(
                portion,
                (
                    (0, 0),
                    (row_half, 1 - row_half),
                    (0, 0),
                    (col_half, 1 - col_half),
                    (0, 0),
                    (0, 0),
                ),
            )
            total_tile = total_tile + portion
    return total_tile.reshape(batch_size, 2 * row_count + 2, 2 * col_count + 2, outward)


def per_device(fields, norm_gain, w_qkv, w_out, conv_weight, conv_bias):
    batch_size, rows_dev, cols_dev, width = fields.shape
    head_count = HEADS
    depth = width // head_count
    seq_count = batch_size * rows_dev
    full = lax.all_gather(fields, "lon", axis=2, tiled=True)
    cols_all = full.shape[2]
    normed_loc = normalize(fields, norm_gain).reshape(seq_count, cols_dev, width)
    normed_all = normalize(full, norm_gain).reshape(seq_count, cols_all, width)
    w_q = w_qkv[:, :width].reshape(width, head_count, depth)
    w_k = w_qkv[:, width : 2 * width].reshape(width, head_count, depth)
    w_v = w_qkv[:, 2 * width :].reshape(width, head_count, depth)
    qh = jnp.einsum("sld,dhe->shle", normed_loc, w_q, preferred_element_type=jnp.float32)
    kt = jnp.einsum("sld,dhe->shel", normed_all, w_k, preferred_element_type=jnp.float32)
    vh = jnp.einsum("sld,dhe->shle", normed_all, w_v, preferred_element_type=jnp.float32)
    qh = qh.astype(jnp.bfloat16).reshape(seq_count * head_count, cols_dev, depth)
    kt = kt.astype(jnp.bfloat16).reshape(seq_count * head_count, depth, cols_all)
    vh = vh.astype(jnp.bfloat16).reshape(seq_count * head_count, cols_all, depth)
    att = attention(qh, kt, vh, 256)
    attended = (
        att.reshape(seq_count, head_count, cols_dev, depth)
        .transpose(0, 2, 1, 3)
        .reshape(seq_count * cols_dev, width)
    )
    update = jnp.dot(attended, w_out, preferred_element_type=jnp.float32).reshape(fields.shape)
    hidden = (fields.astype(jnp.float32) + update).astype(jnp.bfloat16)
    tiled = tap_tile(hidden, conv_weight)
    edge_cols = jnp.concatenate([tiled[:, :, :1], tiled[:, :, -1:]], axis=2)
    from_cols = extended(edge_cols, (("lon", 2),), 1, True)
    middle = tiled[:, :, 1:-1]
    middle = middle.at[:, :, 0].add(from_cols[:, :, 0]).at[:, :, -1].add(from_cols[:, :, 3])
    edge_rows = jnp.concatenate([middle[:, :1], middle[:, -1:]], axis=1)
    from_rows = extended(edge_rows.astype(jnp.bfloat16), (("lat", 1),), 1, False).astype(
        edge_rows.dtype
    )
    result = middle[:, 1:-1]
    result = result.at[:, 0].add(from_rows[:, 0]).at[:, -1].add(from_rows[:, 3])
    return (result + conv_bias).astype(jnp.bfloat16)


def solution(mesh):
    in_specs = (P(None, "lat", "lon", None), P(), P(), P(), P(), P())
    out_specs = P(None, "lat", "lon", None)
    return jax.shard_map(
        per_device, mesh=mesh, in_specs=in_specs, out_specs=out_specs, check_vma=False
    )
```

```python
import math

import jax
import jax.numpy as jnp
from jax import lax
from jax.experimental import pallas as pl
from jax.experimental.pallas import tpu as pltpu
from jax.sharding import PartitionSpec as P

HEADS = 8
NT_DIMS = (((1,), (1,)), ((), ()))


def normalize(fields, norm_gain):
    values = fields.astype(jnp.float32)
    average = jnp.mean(values, axis=-1, keepdims=True)
    centred = values - average
    variance = jnp.mean(centred * centred, axis=-1, keepdims=True)
    return (centred * lax.rsqrt(variance + 1e-05) * norm_gain).astype(jnp.bfloat16)


def attn_kernel(q_ref, kt_ref, vt_ref, o_ref):
    q = q_ref[0]
    kt = kt_ref[0]
    vt = vt_ref[0]
    depth = q.shape[-1]
    coef = depth ** (-0.5) * math.log2(math.e)
    d = jnp.dot(q, kt, preferred_element_type=jnp.float32)
    m = jnp.max(d, axis=-1, keepdims=True)
    p = jnp.exp2(d * coef - m * coef).astype(jnp.bfloat16)
    ones = jnp.ones((16, vt.shape[-1]), vt.dtype)
    vta = jnp.concatenate([vt, ones], axis=0)
    oa = lax.dot_general(p, vta, NT_DIMS, preferred_element_type=jnp.float32)
    o_ref[0] = (oa[:, :depth] / oa[:, depth : depth + 1]).astype(o_ref.dtype)


def attention(qh, kt, vt, tq):
    items, lq, depth = qh.shape
    lk = kt.shape[-1]
    return pl.pallas_call(
        attn_kernel,
        grid=(items, lq // tq),
        in_specs=[
            pl.BlockSpec((1, tq, depth), lambda i, j: (i, j, 0)),
            pl.BlockSpec((1, depth, lk), lambda i, j: (i, 0, 0)),
            pl.BlockSpec((1, depth, lk), lambda i, j: (i, 0, 0)),
        ],
        out_specs=pl.BlockSpec((1, tq, depth), lambda i, j: (i, j, 0)),
        out_shape=jax.ShapeDtypeStruct((items, lq, depth), jnp.bfloat16),
        compiler_params=pltpu.CompilerParams(vmem_limit_bytes=48 * 1024 * 1024),
    )(qh, kt, vt)


def shift(block, axis, step, periodic):
    count = lax.axis_size(axis)
    pairs = [(i, i + step) for i in range(count) if 0 <= i + step < count]
    if periodic:
        pairs = [(i, (i + step) % count) for i in range(count)]
    return lax.ppermute(block, axis, pairs)


def upsample(hidden, conv_weight, conv_bias):
    batch_size, rows_dev, cols_dev, width = hidden.shape
    outward = conv_weight.shape[-1]
    left = shift(hidden[:, :, -1:], "lon", 1, True)
    right = shift(hidden[:, :, :1], "lon", -1, True)
    ext = jnp.concatenate([left, hidden, right], axis=2)
    above = shift(ext, "lat", 1, False)
    below = shift(ext, "lat", -1, False)
    taps = conv_weight.reshape(width, 4, 4 * outward)

    def tap(rows, r):
        return jnp.einsum(
            "brcd,dk->brck", rows, taps[:, r], preferred_element_type=jnp.float32
        ).reshape(batch_size, rows_dev, cols_dev + 2, 4, outward)

    z_even = tap(ext, 1) + tap(above, 3)
    z_odd = tap(ext, 2) + tap(below, 0)

    def columns(z):
        even = z[:, :, 1:-1, 1] + z[:, :, :-2, 3]
        odd = z[:, :, 1:-1, 2] + z[:, :, 2:, 0]
        return jnp.stack([even, odd], axis=3).reshape(batch_size, rows_dev, 2 * cols_dev, outward)

    out = jnp.stack([columns(z_even), columns(z_odd)], axis=2)
    out = out.reshape(batch_size, 2 * rows_dev, 2 * cols_dev, outward)
    return (out + conv_bias).astype(jnp.bfloat16)


def per_device(fields, norm_gain, w_qkv, w_out, conv_weight, conv_bias):
    batch_size, rows_dev, cols_dev, width = fields.shape
    head_count = HEADS
    depth = width // head_count
    seq_count = batch_size * rows_dev
    full = lax.all_gather(fields, "lon", axis=2, tiled=True)
    cols_all = full.shape[2]
    normed_loc = normalize(fields, norm_gain).reshape(seq_count, cols_dev, width)
    normed_all = normalize(full, norm_gain).reshape(seq_count, cols_all, width)
    w_q = w_qkv[:, :width].reshape(width, head_count, depth)
    w_k = w_qkv[:, width : 2 * width].reshape(width, head_count, depth)
    w_v = w_qkv[:, 2 * width :].reshape(width, head_count, depth)
    qh = jnp.einsum("sld,dhe->shle", normed_loc, w_q, preferred_element_type=jnp.float32)
    kt = jnp.einsum("sld,dhe->shel", normed_all, w_k, preferred_element_type=jnp.float32)
    vt = jnp.einsum("sld,dhe->shel", normed_all, w_v, preferred_element_type=jnp.float32)
    qh = qh.astype(jnp.bfloat16).reshape(seq_count * head_count, cols_dev, depth)
    kt = kt.astype(jnp.bfloat16).reshape(seq_count * head_count, depth, cols_all)
    vt = vt.astype(jnp.bfloat16).reshape(seq_count * head_count, depth, cols_all)
    att = attention(qh, kt, vt, cols_dev)
    attended = (
        att.reshape(seq_count, head_count, cols_dev, depth)
        .transpose(0, 2, 1, 3)
        .reshape(seq_count * cols_dev, width)
    )
    update = jnp.dot(attended, w_out, preferred_element_type=jnp.float32).reshape(fields.shape)
    hidden = (fields.astype(jnp.float32) + update).astype(jnp.bfloat16)
    return upsample(hidden, conv_weight, conv_bias)


def solution(mesh):
    in_specs = (P(None, "lat", "lon", None), P(), P(), P(), P(), P())
    out_specs = P(None, "lat", "lon", None)
    return jax.shard_map(
        per_device, mesh=mesh, in_specs=in_specs, out_specs=out_specs, check_vma=False
    )
```

```python
import functools
import math

import jax
import jax.numpy as jnp
from jax import lax
from jax.experimental import pallas as pl
from jax.experimental.pallas import tpu as pltpu
from jax.sharding import PartitionSpec as P

HEADS = 8
NT_DIMS = (((1,), (1,)), ((), ()))


def normalize(fields, norm_gain):
    values = fields.astype(jnp.float32)
    average = jnp.mean(values, axis=-1, keepdims=True)
    centred = values - average
    variance = jnp.mean(centred * centred, axis=-1, keepdims=True)
    return (centred * lax.rsqrt(variance + 1e-05) * norm_gain).astype(jnp.bfloat16)


def chunk_kernel(first, q_ref, kt_ref, vt_ref, *refs):
    if first:
        m_out, acc_out = refs
    else:
        m_in, acc_in, m_out, acc_out = refs
    q = q_ref[0]
    kt = kt_ref[0]
    vt = vt_ref[0]
    coef = q.shape[-1] ** (-0.5) * math.log2(math.e)
    d = jnp.dot(q, kt, preferred_element_type=jnp.float32)
    m = jnp.max(d, axis=-1, keepdims=True)
    if not first:
        m_old = m_in[0]
        m = jnp.maximum(m, m_old)
    p = jnp.exp2(d * coef - m * coef).astype(jnp.bfloat16)
    ones = jnp.ones((16, vt.shape[-1]), vt.dtype)
    vta = jnp.concatenate([vt, ones], axis=0)
    acc = lax.dot_general(p, vta, NT_DIMS, preferred_element_type=jnp.float32)
    if not first:
        acc = acc + acc_in[0] * jnp.exp2((m_old - m) * coef)
    m_out[0] = m
    acc_out[0] = acc


def attend_chunk(qh, kt, vt, state=None):
    items, lq, depth = qh.shape
    lk = kt.shape[-1]
    wide = depth + 16
    first = state is None
    row_spec = pl.BlockSpec((1, lq, 1), lambda i: (i, 0, 0))
    acc_spec = pl.BlockSpec((1, lq, wide), lambda i: (i, 0, 0))
    in_specs = [
        pl.BlockSpec((1, lq, depth), lambda i: (i, 0, 0)),
        pl.BlockSpec((1, depth, lk), lambda i: (i, 0, 0)),
        pl.BlockSpec((1, depth, lk), lambda i: (i, 0, 0)),
    ]
    args = (qh, kt, vt)
    if not first:
        in_specs += [row_spec, acc_spec]
        args += tuple(state)
    return pl.pallas_call(
        functools.partial(chunk_kernel, first),
        grid=(items,),
        in_specs=in_specs,
        out_specs=[row_spec, acc_spec],
        out_shape=[
            jax.ShapeDtypeStruct((items, lq, 1), jnp.float32),
            jax.ShapeDtypeStruct((items, lq, wide), jnp.float32),
        ],
        compiler_params=pltpu.CompilerParams(vmem_limit_bytes=48 * 1024 * 1024),
    )(*args)


def shift(block, axis, step, periodic):
    count = lax.axis_size(axis)
    pairs = [(i, i + step) for i in range(count) if 0 <= i + step < count]
    if periodic:
        pairs = [(i, (i + step) % count) for i in range(count)]
    return lax.ppermute(block, axis, pairs)


def upsample(hidden, conv_weight, conv_bias):
    batch_size, rows_dev, cols_dev, width = hidden.shape
    outward = conv_weight.shape[-1]
    left = shift(hidden[:, :, -1:], "lon", 1, True)
    right = shift(hidden[:, :, :1], "lon", -1, True)
    ext = jnp.concatenate([left, hidden, right], axis=2)
    above = shift(ext, "lat", 1, False)
    below = shift(ext, "lat", -1, False)
    taps = conv_weight.reshape(width, 4, 4 * outward)

    def tap(rows, r):
        return jnp.einsum(
            "brcd,dk->brck", rows, taps[:, r], preferred_element_type=jnp.float32
        ).reshape(batch_size, rows_dev, cols_dev + 2, 4, outward)

    z_even = tap(ext, 1) + tap(above, 3)
    z_odd = tap(ext, 2) + tap(below, 0)

    def columns(z):
        even = z[:, :, 1:-1, 1] + z[:, :, :-2, 3]
        odd = z[:, :, 1:-1, 2] + z[:, :, 2:, 0]
        return jnp.stack([even, odd], axis=3).reshape(batch_size, rows_dev, 2 * cols_dev, outward)

    out = jnp.stack([columns(z_even), columns(z_odd)], axis=2)
    out = out.reshape(batch_size, 2 * rows_dev, 2 * cols_dev, outward)
    return (out + conv_bias).astype(jnp.bfloat16)


def per_device(fields, norm_gain, w_qkv, w_out, conv_weight, conv_bias):
    batch_size, rows_dev, cols_dev, width = fields.shape
    head_count = HEADS
    depth = width // head_count
    seq_count = batch_size * rows_dev
    half = cols_dev // 2
    from_left = shift(fields, "lon", 1, True)
    from_right = shift(fields, "lon", -1, True)
    opposite = jnp.concatenate(
        [
            shift(from_left[:, :, :half], "lon", 1, True),
            shift(from_right[:, :, half:], "lon", -1, True),
        ],
        axis=2,
    )
    w_q = w_qkv[:, :width].reshape(width, head_count, depth)
    w_k = w_qkv[:, width : 2 * width].reshape(width, head_count, depth)
    w_v = w_qkv[:, 2 * width :].reshape(width, head_count, depth)

    def keys_values(chunk):
        normed = normalize(chunk, norm_gain).reshape(seq_count, cols_dev, width)
        kt = jnp.einsum("sld,dhe->shel", normed, w_k, preferred_element_type=jnp.float32)
        vt = jnp.einsum("sld,dhe->shel", normed, w_v, preferred_element_type=jnp.float32)
        shape = (seq_count * head_count, depth, cols_dev)
        return kt.astype(jnp.bfloat16).reshape(shape), vt.astype(jnp.bfloat16).reshape(shape)

    normed_loc = normalize(fields, norm_gain).reshape(seq_count, cols_dev, width)
    qh = jnp.einsum("sld,dhe->shle", normed_loc, w_q, preferred_element_type=jnp.float32)
    qh = qh.astype(jnp.bfloat16).reshape(seq_count * head_count, cols_dev, depth)
    state = attend_chunk(qh, *keys_values(fields))
    for chunk in (from_left, from_right, opposite):
        state = attend_chunk(qh, *keys_values(chunk), state)
    acc = state[1]
    att = acc[..., :depth] / acc[..., depth : depth + 1]
    attended = (
        att.astype(jnp.bfloat16)
        .reshape(seq_count, head_count, cols_dev, depth)
        .transpose(0, 2, 1, 3)
        .reshape(seq_count * cols_dev, width)
    )
    update = jnp.dot(attended, w_out, preferred_element_type=jnp.float32).reshape(fields.shape)
    hidden = (fields.astype(jnp.float32) + update).astype(jnp.bfloat16)
    return upsample(hidden, conv_weight, conv_bias)


def solution(mesh):
    in_specs = (P(None, "lat", "lon", None), P(), P(), P(), P(), P())
    out_specs = P(None, "lat", "lon", None)
    return jax.shard_map(
        per_device, mesh=mesh, in_specs=in_specs, out_specs=out_specs, check_vma=False
    )
```

```python
import functools
import math

import jax
import jax.numpy as jnp
from jax import lax
from jax.experimental import pallas as pl
from jax.experimental.pallas import tpu as pltpu
from jax.sharding import PartitionSpec as P

HEADS = 8
NT_DIMS = (((1,), (1,)), ((), ()))


def normalize(fields, norm_gain):
    values = fields.astype(jnp.float32)
    average = jnp.mean(values, axis=-1, keepdims=True)
    centred = values - average
    variance = jnp.mean(centred * centred, axis=-1, keepdims=True)
    return (centred * lax.rsqrt(variance + 1e-05) * norm_gain).astype(jnp.bfloat16)


def chunk_kernel(first, q_ref, kt_ref, vt_ref, *refs):
    if first:
        m_out, acc_out = refs
    else:
        m_in, acc_in, m_out, acc_out = refs
    q = q_ref[0]
    kt = kt_ref[0]
    vt = vt_ref[0]
    coef = q.shape[-1] ** (-0.5) * math.log2(math.e)
    d = jnp.dot(q, kt, preferred_element_type=jnp.float32)
    m = jnp.max(d, axis=-1, keepdims=True)
    if not first:
        m_old = m_in[0]
        m = jnp.maximum(m, m_old)
    p = jnp.exp2(d * coef - m * coef).astype(jnp.bfloat16)
    ones = jnp.ones((16, vt.shape[-1]), vt.dtype)
    vta = jnp.concatenate([vt, ones], axis=0)
    acc = lax.dot_general(p, vta, NT_DIMS, preferred_element_type=jnp.float32)
    if not first:
        acc = acc + acc_in[0] * jnp.exp2((m_old - m) * coef)
    m_out[0] = m
    acc_out[0] = acc


def attend_chunk(qh, kt, vt, state=None):
    items, lq, depth = qh.shape
    lk = kt.shape[-1]
    wide = depth + 16
    first = state is None
    row_spec = pl.BlockSpec((1, lq, 1), lambda i: (i, 0, 0))
    acc_spec = pl.BlockSpec((1, lq, wide), lambda i: (i, 0, 0))
    in_specs = [
        pl.BlockSpec((1, lq, depth), lambda i: (i, 0, 0)),
        pl.BlockSpec((1, depth, lk), lambda i: (i, 0, 0)),
        pl.BlockSpec((1, depth, lk), lambda i: (i, 0, 0)),
    ]
    args = (qh, kt, vt)
    if not first:
        in_specs += [row_spec, acc_spec]
        args += tuple(state)
    return pl.pallas_call(
        functools.partial(chunk_kernel, first),
        grid=(items,),
        in_specs=in_specs,
        out_specs=[row_spec, acc_spec],
        out_shape=[
            jax.ShapeDtypeStruct((items, lq, 1), jnp.float32),
            jax.ShapeDtypeStruct((items, lq, wide), jnp.float32),
        ],
        compiler_params=pltpu.CompilerParams(vmem_limit_bytes=48 * 1024 * 1024),
    )(*args)


def shift(block, axis, step, periodic):
    count = lax.axis_size(axis)
    pairs = [(i, i + step) for i in range(count) if 0 <= i + step < count]
    if periodic:
        pairs = [(i, (i + step) % count) for i in range(count)]
    return lax.ppermute(block, axis, pairs)


def upsample(ext, conv_weight, conv_bias):
    batch_size, rows_dev, cols_ext, width = ext.shape
    cols_dev = cols_ext - 2
    outward = conv_weight.shape[-1]
    above = shift(ext, "lat", 1, False)
    below = shift(ext, "lat", -1, False)
    taps = conv_weight.reshape(width, 4, 4 * outward)

    def tap(rows, r):
        return jnp.einsum(
            "brcd,dk->brck", rows, taps[:, r], preferred_element_type=jnp.float32
        ).reshape(batch_size, rows_dev, cols_dev + 2, 4, outward)

    z_even = tap(ext, 1) + tap(above, 3)
    z_odd = tap(ext, 2) + tap(below, 0)

    def columns(z):
        even = z[:, :, 1:-1, 1] + z[:, :, :-2, 3]
        odd = z[:, :, 1:-1, 2] + z[:, :, 2:, 0]
        return jnp.stack([even, odd], axis=3).reshape(batch_size, rows_dev, 2 * cols_dev, outward)

    out = jnp.stack([columns(z_even), columns(z_odd)], axis=2)
    out = out.reshape(batch_size, 2 * rows_dev, 2 * cols_dev, outward)
    return (out + conv_bias).astype(jnp.bfloat16)


def per_device(fields, norm_gain, w_qkv, w_out, conv_weight, conv_bias):
    batch_size, rows_dev, cols_dev, width = fields.shape
    head_count = HEADS
    depth = width // head_count
    seq_count = batch_size * rows_dev
    half = cols_dev // 2
    from_left = shift(fields, "lon", 1, True)
    from_right = shift(fields, "lon", -1, True)
    opposite = jnp.concatenate(
        [
            shift(from_left[:, :, :half], "lon", 1, True),
            shift(from_right[:, :, half:], "lon", -1, True),
        ],
        axis=2,
    )
    w_q = w_qkv[:, :width].reshape(width, head_count, depth)
    w_k = w_qkv[:, width : 2 * width].reshape(width, head_count, depth)
    w_v = w_qkv[:, 2 * width :].reshape(width, head_count, depth)

    def keys_values(chunk):
        count = chunk.shape[2]
        normed = normalize(chunk, norm_gain).reshape(seq_count, count, width)
        kt = jnp.einsum("sld,dhe->shel", normed, w_k, preferred_element_type=jnp.float32)
        vt = jnp.einsum("sld,dhe->shel", normed, w_v, preferred_element_type=jnp.float32)
        shape = (seq_count * head_count, depth, count)
        return kt.astype(jnp.bfloat16).reshape(shape), vt.astype(jnp.bfloat16).reshape(shape)

    normed_loc = normalize(fields, norm_gain).reshape(seq_count, cols_dev, width)
    qh = jnp.einsum("sld,dhe->shle", normed_loc, w_q, preferred_element_type=jnp.float32)
    qh = qh.astype(jnp.bfloat16).reshape(seq_count * head_count, cols_dev, depth)
    local_kv = keys_values(fields)
    state = attend_chunk(qh, *local_kv)
    near = jnp.concatenate([from_left, from_right], axis=2)
    near_kv = keys_values(near)
    state = attend_chunk(qh, *near_kv, state)
    opposite_kv = keys_values(opposite)
    state = attend_chunk(qh, *opposite_kv, state)

    pad = 8
    edge = jnp.concatenate(
        [from_left[:, :, -1:], from_right[:, :, :1], jnp.zeros_like(fields[:, :, : pad - 2])],
        axis=2,
    )
    normed_edge = normalize(edge, norm_gain).reshape(seq_count, pad, width)
    q_edge = jnp.einsum("sld,dhe->shle", normed_edge, w_q, preferred_element_type=jnp.float32)
    q_edge = q_edge.astype(jnp.bfloat16).reshape(seq_count * head_count, pad, depth)
    kt_all = jnp.concatenate([local_kv[0], near_kv[0], opposite_kv[0]], axis=-1)
    vt_all = jnp.concatenate([local_kv[1], near_kv[1], opposite_kv[1]], axis=-1)
    edge_state = attend_chunk(q_edge, kt_all, vt_all)

    def finish(acc, block, count):
        att = acc[..., :depth] / acc[..., depth : depth + 1]
        attended = (
            att.astype(jnp.bfloat16)
            .reshape(seq_count, head_count, count, depth)
            .transpose(0, 2, 1, 3)
            .reshape(seq_count * count, width)
        )
        update = jnp.dot(attended, w_out, preferred_element_type=jnp.float32)
        update = update.reshape(batch_size, rows_dev, count, width)
        return (block.astype(jnp.float32) + update).astype(jnp.bfloat16)

    hidden = finish(state[1], fields, cols_dev)
    hidden_edge = finish(edge_state[1], edge, pad)
    ext = jnp.concatenate([hidden_edge[:, :, :1], hidden, hidden_edge[:, :, 1:2]], axis=2)
    return upsample(ext, conv_weight, conv_bias)


def solution(mesh):
    in_specs = (P(None, "lat", "lon", None), P(), P(), P(), P(), P())
    out_specs = P(None, "lat", "lon", None)
    return jax.shard_map(
        per_device, mesh=mesh, in_specs=in_specs, out_specs=out_specs, check_vma=False
    )
```

```python
import functools
import math

import jax
import jax.numpy as jnp
from jax import lax
from jax.experimental import pallas as pl
from jax.experimental.pallas import tpu as pltpu
from jax.sharding import PartitionSpec as P

HEADS = 8
NT_DIMS = (((1,), (1,)), ((), ()))


def normalize(fields, norm_gain):
    values = fields.astype(jnp.float32)
    average = jnp.mean(values, axis=-1, keepdims=True)
    centred = values - average
    variance = jnp.mean(centred * centred, axis=-1, keepdims=True)
    return (centred * lax.rsqrt(variance + 1e-05) * norm_gain).astype(jnp.bfloat16)


def chunk_kernel(first, last, q_ref, kt_ref, vt_ref, *refs):
    if first:
        m_out, acc_out = refs
    elif last:
        m_in, acc_in, o_out = refs
    else:
        m_in, acc_in, m_out, acc_out = refs
    q = q_ref[0]
    kt = kt_ref[0]
    vt = vt_ref[0]
    coef = q.shape[-1] ** (-0.5) * math.log2(math.e)
    d = jnp.dot(q, kt, preferred_element_type=jnp.float32)
    m = jnp.max(d, axis=-1, keepdims=True)
    if not first:
        m_old = m_in[0]
        m = jnp.maximum(m, m_old)
    p = jnp.exp2(d * coef - m * coef).astype(jnp.bfloat16)
    ones = jnp.ones((16, vt.shape[-1]), vt.dtype)
    vta = jnp.concatenate([vt, ones], axis=0)
    acc = lax.dot_general(p, vta, NT_DIMS, preferred_element_type=jnp.float32)
    if not first:
        acc = acc + acc_in[0] * jnp.exp2((m_old - m) * coef)
    depth = q.shape[-1]
    if last:
        o_out[0] = (acc[:, :depth] / acc[:, depth : depth + 1]).astype(o_out.dtype)
    else:
        m_out[0] = m
        acc_out[0] = acc


def edge_kernel(q_ref, *refs):
    *kv_refs, o_ref = refs
    count = len(kv_refs) // 2
    coef = q_ref.shape[-1] ** (-0.5) * math.log2(math.e)
    depth = q_ref.shape[-1]
    for i in range(q_ref.shape[0]):
        q = q_ref[i]
        kt = jnp.concatenate([r[i] for r in kv_refs[:count]], axis=-1)
        vt = jnp.concatenate([r[i] for r in kv_refs[count:]], axis=-1)
        d = jnp.dot(q, kt, preferred_element_type=jnp.float32)
        m = jnp.max(d, axis=-1, keepdims=True)
        p = jnp.exp2(d * coef - m * coef).astype(jnp.bfloat16)
        ones = jnp.ones((16, vt.shape[-1]), vt.dtype)
        vta = jnp.concatenate([vt, ones], axis=0)
        acc = lax.dot_general(p, vta, NT_DIMS, preferred_element_type=jnp.float32)
        o_ref[i] = (acc[:, :depth] / acc[:, depth : depth + 1]).astype(o_ref.dtype)


def attend_edge(q, kts, vts):
    return pl.pallas_call(
        edge_kernel,
        out_shape=jax.ShapeDtypeStruct(q.shape, jnp.bfloat16),
        compiler_params=pltpu.CompilerParams(vmem_limit_bytes=48 * 1024 * 1024),
    )(q, *kts, *vts)


def attend_chunk(qh, kt, vt, state=None, last=False):
    items, lq, depth = qh.shape
    lk = kt.shape[-1]
    wide = depth + 16
    first = state is None
    row_spec = pl.BlockSpec((1, lq, 1), lambda i: (i, 0, 0))
    acc_spec = pl.BlockSpec((1, lq, wide), lambda i: (i, 0, 0))
    in_specs = [
        pl.BlockSpec((1, lq, depth), lambda i: (i, 0, 0)),
        pl.BlockSpec((1, depth, lk), lambda i: (i, 0, 0)),
        pl.BlockSpec((1, depth, lk), lambda i: (i, 0, 0)),
    ]
    args = (qh, kt, vt)
    if not first:
        in_specs += [row_spec, acc_spec]
        args += tuple(state)
    out_specs = [row_spec, acc_spec]
    out_shape = [
        jax.ShapeDtypeStruct((items, lq, 1), jnp.float32),
        jax.ShapeDtypeStruct((items, lq, wide), jnp.float32),
    ]
    if last:
        out_specs = pl.BlockSpec((1, lq, depth), lambda i: (i, 0, 0))
        out_shape = jax.ShapeDtypeStruct((items, lq, depth), jnp.bfloat16)
    return pl.pallas_call(
        functools.partial(chunk_kernel, first, last),
        grid=(items,),
        in_specs=in_specs,
        out_specs=out_specs,
        out_shape=out_shape,
        compiler_params=pltpu.CompilerParams(vmem_limit_bytes=48 * 1024 * 1024),
    )(*args)


def shift(block, axis, step, periodic):
    count = lax.axis_size(axis)
    pairs = [(i, i + step) for i in range(count) if 0 <= i + step < count]
    if periodic:
        pairs = [(i, (i + step) % count) for i in range(count)]
    return lax.ppermute(block, axis, pairs)


def upsample(ext, conv_weight, conv_bias):
    batch_size, rows_dev, cols_ext, width = ext.shape
    cols_dev = cols_ext - 2
    outward = conv_weight.shape[-1]
    above = shift(ext, "lat", 1, False)
    below = shift(ext, "lat", -1, False)
    taps = conv_weight.reshape(width, 4, 4 * outward)

    def tap(rows, r):
        return jnp.einsum(
            "brcd,dk->brck", rows, taps[:, r], preferred_element_type=jnp.float32
        ).reshape(batch_size, rows_dev, cols_dev + 2, 4, outward)

    z_even = tap(ext, 1) + tap(above, 3)
    z_odd = tap(ext, 2) + tap(below, 0)

    def columns(z):
        even = z[:, :, 1:-1, 1] + z[:, :, :-2, 3]
        odd = z[:, :, 1:-1, 2] + z[:, :, 2:, 0]
        return jnp.stack([even, odd], axis=3).reshape(batch_size, rows_dev, 2 * cols_dev, outward)

    out = jnp.stack([columns(z_even), columns(z_odd)], axis=2)
    out = out.reshape(batch_size, 2 * rows_dev, 2 * cols_dev, outward)
    return (out + conv_bias).astype(jnp.bfloat16)


def per_device(fields, norm_gain, w_qkv, w_out, conv_weight, conv_bias):
    batch_size, rows_dev, cols_dev, width = fields.shape
    head_count = HEADS
    depth = width // head_count
    seq_count = batch_size * rows_dev
    half = cols_dev // 2
    from_left = shift(fields, "lon", 1, True)
    from_right = shift(fields, "lon", -1, True)
    opposite = jnp.concatenate(
        [
            shift(from_left[:, :, :half], "lon", 1, True),
            shift(from_right[:, :, half:], "lon", -1, True),
        ],
        axis=2,
    )
    w_q = w_qkv[:, :width].reshape(width, head_count, depth)
    w_k = w_qkv[:, width : 2 * width].reshape(width, head_count, depth)
    w_v = w_qkv[:, 2 * width :].reshape(width, head_count, depth)

    def keys_values(chunk):
        count = chunk.shape[2]
        normed = normalize(chunk, norm_gain).reshape(seq_count, count, width)
        kt = jnp.einsum("sld,dhe->shel", normed, w_k, preferred_element_type=jnp.float32)
        vt = jnp.einsum("sld,dhe->shel", normed, w_v, preferred_element_type=jnp.float32)
        shape = (seq_count * head_count, depth, count)
        return kt.astype(jnp.bfloat16).reshape(shape), vt.astype(jnp.bfloat16).reshape(shape)

    normed_loc = normalize(fields, norm_gain).reshape(seq_count, cols_dev, width)
    qh = jnp.einsum("sld,dhe->shle", normed_loc, w_q, preferred_element_type=jnp.float32)
    qh = qh.astype(jnp.bfloat16).reshape(seq_count * head_count, cols_dev, depth)
    local_kv = keys_values(fields)
    state = attend_chunk(qh, *local_kv)
    near = jnp.concatenate([from_left, from_right], axis=2)
    near_kv = keys_values(near)
    state = attend_chunk(qh, *near_kv, state)
    opposite_kv = keys_values(opposite)
    att = attend_chunk(qh, *opposite_kv, state, last=True)

    pad = 8
    edge = jnp.concatenate(
        [from_left[:, :, -1:], from_right[:, :, :1], jnp.zeros_like(fields[:, :, : pad - 2])],
        axis=2,
    )
    normed_edge = normalize(edge, norm_gain).reshape(seq_count, pad, width)
    q_edge = jnp.einsum("sld,dhe->shle", normed_edge, w_q, preferred_element_type=jnp.float32)
    q_edge = q_edge.astype(jnp.bfloat16).reshape(seq_count * head_count, pad, depth)
    parts = (local_kv, near_kv, opposite_kv)
    att_edge = attend_edge(q_edge, [kv[0] for kv in parts], [kv[1] for kv in parts])

    def finish(att, block, count):
        attended = (
            att.reshape(seq_count, head_count, count, depth)
            .transpose(0, 2, 1, 3)
            .reshape(seq_count * count, width)
        )
        update = jnp.dot(attended, w_out, preferred_element_type=jnp.float32)
        update = update.reshape(batch_size, rows_dev, count, width)
        return (block.astype(jnp.float32) + update).astype(jnp.bfloat16)

    hidden = finish(att, fields, cols_dev)
    hidden_edge = finish(att_edge, edge, pad)
    ext = jnp.concatenate([hidden_edge[:, :, :1], hidden, hidden_edge[:, :, 1:2]], axis=2)
    return upsample(ext, conv_weight, conv_bias)


def solution(mesh):
    in_specs = (P(None, "lat", "lon", None), P(), P(), P(), P(), P())
    out_specs = P(None, "lat", "lon", None)
    return jax.shard_map(
        per_device, mesh=mesh, in_specs=in_specs, out_specs=out_specs, check_vma=False
    )
```

```python
import functools
import math

import jax
import jax.numpy as jnp
from jax import lax
from jax.experimental import pallas as pl
from jax.experimental.pallas import tpu as pltpu
from jax.sharding import PartitionSpec as P

HEADS = 8
NT_DIMS = (((1,), (1,)), ((), ()))


def normalize(fields, norm_gain):
    values = fields.astype(jnp.float32)
    average = jnp.mean(values, axis=-1, keepdims=True)
    centred = values - average
    variance = jnp.mean(centred * centred, axis=-1, keepdims=True)
    return (centred * lax.rsqrt(variance + 1e-05) * norm_gain).astype(jnp.bfloat16)


def chunk_kernel(first, last, parts, q_ref, *refs):
    kt_refs, vt_refs, refs = refs[:parts], refs[parts : 2 * parts], refs[2 * parts :]
    if first:
        m_out, acc_out = refs
    elif last:
        m_in, acc_in, o_out = refs
    else:
        m_in, acc_in, m_out, acc_out = refs
    q = q_ref[0]
    kt = jnp.concatenate([r[0] for r in kt_refs], axis=-1)
    vt = jnp.concatenate([r[0] for r in vt_refs], axis=-1)
    coef = q.shape[-1] ** (-0.5) * math.log2(math.e)
    d = jnp.dot(q, kt, preferred_element_type=jnp.float32)
    m = jnp.max(d, axis=-1, keepdims=True)
    if not first:
        m_old = m_in[0]
        m = jnp.maximum(m, m_old)
    p = jnp.exp2(d * coef - m * coef).astype(jnp.bfloat16)
    ones = jnp.ones((16, vt.shape[-1]), vt.dtype)
    vta = jnp.concatenate([vt, ones], axis=0)
    acc = lax.dot_general(p, vta, NT_DIMS, preferred_element_type=jnp.float32)
    if not first:
        acc = acc + acc_in[0] * jnp.exp2((m_old - m) * coef)
    depth = q.shape[-1]
    if last:
        o_out[0] = (acc[:, :depth] / acc[:, depth : depth + 1]).astype(o_out.dtype)
    else:
        m_out[0] = m
        acc_out[0] = acc


def edge_kernel(q_ref, *refs):
    *kv_refs, o_ref = refs
    count = len(kv_refs) // 2
    coef = q_ref.shape[-1] ** (-0.5) * math.log2(math.e)
    depth = q_ref.shape[-1]
    for i in range(q_ref.shape[0]):
        q = q_ref[i]
        kt = jnp.concatenate([r[i] for r in kv_refs[:count]], axis=-1)
        vt = jnp.concatenate([r[i] for r in kv_refs[count:]], axis=-1)
        d = jnp.dot(q, kt, preferred_element_type=jnp.float32)
        m = jnp.max(d, axis=-1, keepdims=True)
        p = jnp.exp2(d * coef - m * coef).astype(jnp.bfloat16)
        ones = jnp.ones((16, vt.shape[-1]), vt.dtype)
        vta = jnp.concatenate([vt, ones], axis=0)
        acc = lax.dot_general(p, vta, NT_DIMS, preferred_element_type=jnp.float32)
        o_ref[i] = (acc[:, :depth] / acc[:, depth : depth + 1]).astype(o_ref.dtype)


def attend_edge(q, kts, vts):
    return pl.pallas_call(
        edge_kernel,
        out_shape=jax.ShapeDtypeStruct(q.shape, jnp.bfloat16),
        compiler_params=pltpu.CompilerParams(vmem_limit_bytes=48 * 1024 * 1024),
    )(q, *kts, *vts)


def attend_chunk(qh, kts, vts, state=None, last=False):
    items, lq, depth = qh.shape
    wide = depth + 16
    first = state is None
    row_spec = pl.BlockSpec((1, lq, 1), lambda i: (i, 0, 0))
    acc_spec = pl.BlockSpec((1, lq, wide), lambda i: (i, 0, 0))
    in_specs = [pl.BlockSpec((1, lq, depth), lambda i: (i, 0, 0))]
    in_specs += [pl.BlockSpec((1, depth, t.shape[-1]), lambda i: (i, 0, 0)) for t in kts]
    in_specs += [pl.BlockSpec((1, depth, t.shape[-1]), lambda i: (i, 0, 0)) for t in vts]
    args = (qh, *kts, *vts)
    if not first:
        in_specs += [row_spec, acc_spec]
        args += tuple(state)
    out_specs = [row_spec, acc_spec]
    out_shape = [
        jax.ShapeDtypeStruct((items, lq, 1), jnp.float32),
        jax.ShapeDtypeStruct((items, lq, wide), jnp.float32),
    ]
    if last:
        out_specs = pl.BlockSpec((1, lq, depth), lambda i: (i, 0, 0))
        out_shape = jax.ShapeDtypeStruct((items, lq, depth), jnp.bfloat16)
    return pl.pallas_call(
        functools.partial(chunk_kernel, first, last, len(kts)),
        grid=(items,),
        in_specs=in_specs,
        out_specs=out_specs,
        out_shape=out_shape,
        compiler_params=pltpu.CompilerParams(vmem_limit_bytes=48 * 1024 * 1024),
    )(*args)


def shift(block, axis, step, periodic):
    count = lax.axis_size(axis)
    pairs = [(i, i + step) for i in range(count) if 0 <= i + step < count]
    if periodic:
        pairs = [(i, (i + step) % count) for i in range(count)]
    return lax.ppermute(block, axis, pairs)


def upsample(ext, conv_weight, conv_bias):
    batch_size, rows_dev, cols_ext, width = ext.shape
    cols_dev = cols_ext - 2
    outward = conv_weight.shape[-1]
    above = shift(ext, "lat", 1, False)
    below = shift(ext, "lat", -1, False)
    taps = conv_weight.reshape(width, 4, 4 * outward)

    def tap(rows, r):
        return jnp.einsum(
            "brcd,dk->brck", rows, taps[:, r], preferred_element_type=jnp.float32
        ).reshape(batch_size, rows_dev, cols_dev + 2, 4, outward)

    z_even = tap(ext, 1) + tap(above, 3)
    z_odd = tap(ext, 2) + tap(below, 0)

    def columns(z):
        even = z[:, :, 1:-1, 1] + z[:, :, :-2, 3]
        odd = z[:, :, 1:-1, 2] + z[:, :, 2:, 0]
        return jnp.stack([even, odd], axis=3).reshape(batch_size, rows_dev, 2 * cols_dev, outward)

    out = jnp.stack([columns(z_even), columns(z_odd)], axis=2)
    out = out.reshape(batch_size, 2 * rows_dev, 2 * cols_dev, outward)
    return (out + conv_bias).astype(jnp.bfloat16)


def per_device(fields, norm_gain, w_qkv, w_out, conv_weight, conv_bias):
    batch_size, rows_dev, cols_dev, width = fields.shape
    head_count = HEADS
    depth = width // head_count
    seq_count = batch_size * rows_dev
    half = cols_dev // 2
    from_left = shift(fields, "lon", 1, True)
    from_right = shift(fields, "lon", -1, True)
    opposite = jnp.concatenate(
        [
            shift(from_left[:, :, :half], "lon", 1, True),
            shift(from_right[:, :, half:], "lon", -1, True),
        ],
        axis=2,
    )
    w_q = w_qkv[:, :width].reshape(width, head_count, depth)
    w_k = w_qkv[:, width : 2 * width].reshape(width, head_count, depth)
    w_v = w_qkv[:, 2 * width :].reshape(width, head_count, depth)

    def keys_values(chunk):
        count = chunk.shape[2]
        normed = normalize(chunk, norm_gain).reshape(seq_count, count, width)
        kt = jnp.einsum("sld,dhe->shel", normed, w_k, preferred_element_type=jnp.float32)
        vt = jnp.einsum("sld,dhe->shel", normed, w_v, preferred_element_type=jnp.float32)
        shape = (seq_count * head_count, depth, count)
        return kt.astype(jnp.bfloat16).reshape(shape), vt.astype(jnp.bfloat16).reshape(shape)

    def queries(block):
        count = block.shape[2]
        normed = normalize(block, norm_gain).reshape(seq_count, count, width)
        qh = jnp.einsum("sld,dhe->shle", normed, w_q, preferred_element_type=jnp.float32)
        return qh.astype(jnp.bfloat16).reshape(seq_count * head_count, count, depth)

    pad = 8
    edge = jnp.concatenate(
        [from_left[:, :, -1:], from_right[:, :, :1], jnp.zeros_like(fields[:, :, : pad - 2])],
        axis=2,
    )
    qh = jnp.concatenate([queries(fields), queries(edge)], axis=1)
    local_kv = keys_values(fields)
    near_kv = keys_values(jnp.concatenate([from_left, from_right], axis=2))
    state = attend_chunk(qh, [near_kv[0]], [near_kv[1]])
    opposite_kv = keys_values(opposite)
    att_all = attend_chunk(
        qh, [opposite_kv[0], local_kv[0]], [opposite_kv[1], local_kv[1]], state, last=True
    )
    att = att_all[:, :cols_dev]
    att_edge = att_all[:, cols_dev:]

    def finish(att, block, count):
        attended = (
            att.reshape(seq_count, head_count, count, depth)
            .transpose(0, 2, 1, 3)
            .reshape(seq_count * count, width)
        )
        update = jnp.dot(attended, w_out, preferred_element_type=jnp.float32)
        update = update.reshape(batch_size, rows_dev, count, width)
        return (block.astype(jnp.float32) + update).astype(jnp.bfloat16)

    hidden = finish(att, fields, cols_dev)
    hidden_edge = finish(att_edge, edge, pad)
    ext = jnp.concatenate([hidden_edge[:, :, :1], hidden, hidden_edge[:, :, 1:2]], axis=2)
    return upsample(ext, conv_weight, conv_bias)


def solution(mesh):
    in_specs = (P(None, "lat", "lon", None), P(), P(), P(), P(), P())
    out_specs = P(None, "lat", "lon", None)
    return jax.shard_map(
        per_device, mesh=mesh, in_specs=in_specs, out_specs=out_specs, check_vma=False
    )
```

```python
import functools
import math

import jax
import jax.numpy as jnp
from jax import lax
from jax.experimental import pallas as pl
from jax.experimental.pallas import tpu as pltpu
from jax.sharding import PartitionSpec as P

HEADS = 8
NT_DIMS = (((1,), (1,)), ((), ()))


def normalize(fields, norm_gain):
    values = fields.astype(jnp.float32)
    average = jnp.mean(values, axis=-1, keepdims=True)
    centred = values - average
    variance = jnp.mean(centred * centred, axis=-1, keepdims=True)
    return (centred * lax.rsqrt(variance + 1e-05) * norm_gain).astype(jnp.bfloat16)


def chunk_kernel(first, last, parts, q_ref, *refs):
    kt_refs, vt_refs, refs = refs[:parts], refs[parts : 2 * parts], refs[2 * parts :]
    if first:
        m_out, acc_out = refs
    elif last:
        m_in, acc_in, o_out, o_edge = refs
    else:
        m_in, acc_in, m_out, acc_out = refs
    q = q_ref[0]
    kt = jnp.concatenate([r[0] for r in kt_refs], axis=-1)
    vt = jnp.concatenate([r[0] for r in vt_refs], axis=-1)
    coef = q.shape[-1] ** (-0.5) * math.log2(math.e)
    d = jnp.dot(q, kt, preferred_element_type=jnp.float32)
    m = jnp.max(d, axis=-1, keepdims=True)
    if not first:
        m_old = m_in[0]
        m = jnp.maximum(m, m_old)
    p = jnp.exp2(d * coef - m * coef).astype(jnp.bfloat16)
    ones = jnp.ones((16, vt.shape[-1]), vt.dtype)
    vta = jnp.concatenate([vt, ones], axis=0)
    acc = lax.dot_general(p, vta, NT_DIMS, preferred_element_type=jnp.float32)
    if not first:
        acc = acc + acc_in[0] * jnp.exp2((m_old - m) * coef)
    depth = q.shape[-1]
    if last:
        o = (acc[:, :depth] / acc[:, depth : depth + 1]).astype(o_out.dtype)
        count = o_out.shape[1]
        o_out[0] = o[:count]
        o_edge[0] = o[count:]
    else:
        m_out[0] = m
        acc_out[0] = acc


def attend_chunk(qh, kts, vts, state=None, last=0):
    items, lq, depth = qh.shape
    wide = depth + 16
    first = state is None
    row_spec = pl.BlockSpec((1, lq, 1), lambda i: (i, 0, 0))
    acc_spec = pl.BlockSpec((1, lq, wide), lambda i: (i, 0, 0))
    in_specs = [pl.BlockSpec((1, lq, depth), lambda i: (i, 0, 0))]
    in_specs += [pl.BlockSpec((1, depth, t.shape[-1]), lambda i: (i, 0, 0)) for t in kts]
    in_specs += [pl.BlockSpec((1, depth, t.shape[-1]), lambda i: (i, 0, 0)) for t in vts]
    args = (qh, *kts, *vts)
    if not first:
        in_specs += [row_spec, acc_spec]
        args += tuple(state)
    out_specs = [row_spec, acc_spec]
    out_shape = [
        jax.ShapeDtypeStruct((items, lq, 1), jnp.float32),
        jax.ShapeDtypeStruct((items, lq, wide), jnp.float32),
    ]
    if last:
        out_specs = [
            pl.BlockSpec((1, lq - last, depth), lambda i: (i, 0, 0)),
            pl.BlockSpec((1, last, depth), lambda i: (i, 0, 0)),
        ]
        out_shape = [
            jax.ShapeDtypeStruct((items, lq - last, depth), jnp.bfloat16),
            jax.ShapeDtypeStruct((items, last, depth), jnp.bfloat16),
        ]
    return pl.pallas_call(
        functools.partial(chunk_kernel, first, last, len(kts)),
        grid=(items,),
        in_specs=in_specs,
        out_specs=out_specs,
        out_shape=out_shape,
        compiler_params=pltpu.CompilerParams(vmem_limit_bytes=48 * 1024 * 1024),
    )(*args)


def shift(block, axis, step, periodic):
    count = lax.axis_size(axis)
    pairs = [(i, i + step) for i in range(count) if 0 <= i + step < count]
    if periodic:
        pairs = [(i, (i + step) % count) for i in range(count)]
    return lax.ppermute(block, axis, pairs)


def upsample(ext, conv_weight, conv_bias):
    batch_size, rows_dev, cols_ext, width = ext.shape
    cols_dev = cols_ext - 2
    outward = conv_weight.shape[-1]
    above = shift(ext, "lat", 1, False)
    below = shift(ext, "lat", -1, False)
    taps = conv_weight.reshape(width, 4, 4 * outward)

    def tap(rows, r):
        return jnp.einsum(
            "brcd,dk->brck", rows, taps[:, r], preferred_element_type=jnp.float32
        ).reshape(batch_size, rows_dev, cols_dev + 2, 4, outward)

    z_even = tap(ext, 1) + tap(above, 3)
    z_odd = tap(ext, 2) + tap(below, 0)

    def columns(z):
        even = z[:, :, 1:-1, 1] + z[:, :, :-2, 3]
        odd = z[:, :, 1:-1, 2] + z[:, :, 2:, 0]
        return jnp.stack([even, odd], axis=3).reshape(batch_size, rows_dev, 2 * cols_dev, outward)

    out = jnp.stack([columns(z_even), columns(z_odd)], axis=2)
    out = out.reshape(batch_size, 2 * rows_dev, 2 * cols_dev, outward)
    return (out + conv_bias).astype(jnp.bfloat16)


def per_device(fields, norm_gain, w_qkv, w_out, conv_weight, conv_bias):
    batch_size, rows_dev, cols_dev, width = fields.shape
    head_count = HEADS
    depth = width // head_count
    seq_count = batch_size * rows_dev
    half = cols_dev // 2
    from_left = shift(fields, "lon", 1, True)
    from_right = shift(fields, "lon", -1, True)
    opposite = jnp.concatenate(
        [
            shift(from_left[:, :, :half], "lon", 1, True),
            shift(from_right[:, :, half:], "lon", -1, True),
        ],
        axis=2,
    )
    w_q = w_qkv[:, :width].reshape(width, head_count, depth)
    w_k = w_qkv[:, width : 2 * width].reshape(width, head_count, depth)
    w_v = w_qkv[:, 2 * width :].reshape(width, head_count, depth)

    def keys_values(chunk):
        count = chunk.shape[2]
        normed = normalize(chunk, norm_gain).reshape(seq_count, count, width)
        kt = jnp.einsum("sld,dhe->shel", normed, w_k, preferred_element_type=jnp.float32)
        vt = jnp.einsum("sld,dhe->shel", normed, w_v, preferred_element_type=jnp.float32)
        shape = (seq_count * head_count, depth, count)
        return kt.astype(jnp.bfloat16).reshape(shape), vt.astype(jnp.bfloat16).reshape(shape)

    def queries(block):
        count = block.shape[2]
        normed = normalize(block, norm_gain).reshape(seq_count, count, width)
        qh = jnp.einsum("sld,dhe->shle", normed, w_q, preferred_element_type=jnp.float32)
        return qh.astype(jnp.bfloat16).reshape(seq_count * head_count, count, depth)

    pad = 16
    edge = jnp.concatenate(
        [from_left[:, :, -1:], from_right[:, :, :1], jnp.zeros_like(fields[:, :, : pad - 2])],
        axis=2,
    )
    qh = jnp.concatenate([queries(fields), queries(edge)], axis=1)
    local_kv = keys_values(fields)
    near_kv = keys_values(jnp.concatenate([from_left, from_right], axis=2))
    state = attend_chunk(qh, [near_kv[0]], [near_kv[1]])
    opposite_kv = keys_values(opposite)
    att, att_edge = attend_chunk(
        qh, [opposite_kv[0], local_kv[0]], [opposite_kv[1], local_kv[1]], state, last=pad
    )

    def finish(att, block, count):
        update = jnp.einsum(
            "shle,hef->slf",
            att.reshape(seq_count, head_count, count, depth),
            w_out.reshape(head_count, depth, width),
            preferred_element_type=jnp.float32,
        )
        update = update.reshape(batch_size, rows_dev, count, width)
        return (block.astype(jnp.float32) + update).astype(jnp.bfloat16)

    hidden = finish(att, fields, cols_dev)
    hidden_edge = finish(att_edge, edge, pad)
    ext = jnp.concatenate([hidden_edge[:, :, :1], hidden, hidden_edge[:, :, 1:2]], axis=2)
    return upsample(ext, conv_weight, conv_bias)


def solution(mesh):
    in_specs = (P(None, "lat", "lon", None), P(), P(), P(), P(), P())
    out_specs = P(None, "lat", "lon", None)
    return jax.shard_map(
        per_device, mesh=mesh, in_specs=in_specs, out_specs=out_specs, check_vma=False
    )
```

```python
import functools
import math

import jax
import jax.numpy as jnp
from jax import lax
from jax.experimental import pallas as pl
from jax.experimental.pallas import tpu as pltpu
from jax.sharding import PartitionSpec as P

HEADS = 8
NT_DIMS = (((1,), (1,)), ((), ()))


def normalize(fields, norm_gain):
    values = fields.astype(jnp.float32)
    average = jnp.mean(values, axis=-1, keepdims=True)
    centred = values - average
    variance = jnp.mean(centred * centred, axis=-1, keepdims=True)
    return (centred * lax.rsqrt(variance + 1e-05) * norm_gain).astype(jnp.bfloat16)


def chunk_kernel(first, last, parts, q_ref, *refs):
    kt_refs, vt_refs, refs = refs[:parts], refs[parts : 2 * parts], refs[2 * parts :]
    if first:
        m_out, acc_out = refs
    elif last:
        m_in, acc_in, o_out, o_edge = refs
    else:
        m_in, acc_in, m_out, acc_out = refs
    q = q_ref[0]
    kt = jnp.concatenate([r[0] for r in kt_refs], axis=-1)
    vt = jnp.concatenate([r[0] for r in vt_refs], axis=-1)
    coef = q.shape[-1] ** (-0.5) * math.log2(math.e)
    d = jnp.dot(q, kt, preferred_element_type=jnp.float32)
    m = jnp.max(d, axis=-1, keepdims=True)
    if not first:
        m_old = m_in[0]
        m = jnp.maximum(m, m_old)
    p = jnp.exp2(d * coef - m * coef).astype(jnp.bfloat16)
    ones = jnp.ones((16, vt.shape[-1]), vt.dtype)
    vta = jnp.concatenate([vt, ones], axis=0)
    acc = lax.dot_general(p, vta, NT_DIMS, preferred_element_type=jnp.float32)
    if not first:
        acc = acc + acc_in[0] * jnp.exp2((m_old - m) * coef)
    depth = q.shape[-1]
    if last:
        o = (acc[:, :depth] / acc[:, depth : depth + 1]).astype(o_out.dtype)
        count = o_out.shape[1]
        o_out[0] = o[:count]
        o_edge[0] = o[count:]
    else:
        m_out[0] = m
        acc_out[0] = acc


def attend_chunk(qh, kts, vts, state=None, last=0):
    items, lq, depth = qh.shape
    wide = depth + 16
    first = state is None
    row_spec = pl.BlockSpec((1, lq, 1), lambda i: (i, 0, 0))
    acc_spec = pl.BlockSpec((1, lq, wide), lambda i: (i, 0, 0))
    in_specs = [pl.BlockSpec((1, lq, depth), lambda i: (i, 0, 0))]
    in_specs += [pl.BlockSpec((1, depth, t.shape[-1]), lambda i: (i, 0, 0)) for t in kts]
    in_specs += [pl.BlockSpec((1, depth, t.shape[-1]), lambda i: (i, 0, 0)) for t in vts]
    args = (qh, *kts, *vts)
    if not first:
        in_specs += [row_spec, acc_spec]
        args += tuple(state)
    out_specs = [row_spec, acc_spec]
    out_shape = [
        jax.ShapeDtypeStruct((items, lq, 1), jnp.float32),
        jax.ShapeDtypeStruct((items, lq, wide), jnp.float32),
    ]
    if last:
        out_specs = [
            pl.BlockSpec((1, lq - last, depth), lambda i: (i, 0, 0)),
            pl.BlockSpec((1, last, depth), lambda i: (i, 0, 0)),
        ]
        out_shape = [
            jax.ShapeDtypeStruct((items, lq - last, depth), jnp.bfloat16),
            jax.ShapeDtypeStruct((items, last, depth), jnp.bfloat16),
        ]
    return pl.pallas_call(
        functools.partial(chunk_kernel, first, last, len(kts)),
        grid=(items,),
        in_specs=in_specs,
        out_specs=out_specs,
        out_shape=out_shape,
        compiler_params=pltpu.CompilerParams(vmem_limit_bytes=48 * 1024 * 1024),
    )(*args)


def shift(block, axis, step, periodic):
    count = lax.axis_size(axis)
    pairs = [(i, i + step) for i in range(count) if 0 <= i + step < count]
    if periodic:
        pairs = [(i, (i + step) % count) for i in range(count)]
    return lax.ppermute(block, axis, pairs)


def upsample(ext, conv_weight, conv_bias):
    batch_size, rows_dev, cols_ext, width = ext.shape
    cols_dev = cols_ext - 2
    outward = conv_weight.shape[-1]
    above = shift(ext, "lat", 1, False)
    below = shift(ext, "lat", -1, False)
    taps = conv_weight.reshape(width, 4, 4 * outward)

    def tap(rows, r):
        return jnp.einsum(
            "brcd,dk->brck", rows, taps[:, r], preferred_element_type=jnp.float32
        ).reshape(batch_size, rows_dev, cols_dev + 2, 4, outward)

    z = jnp.concatenate([tap(ext, 1) + tap(above, 3), tap(ext, 2) + tap(below, 0)], axis=1)
    even = z[:, :, 1:-1, 1] + z[:, :, :-2, 3]
    odd = z[:, :, 1:-1, 2] + z[:, :, 2:, 0]
    out = jnp.stack([even, odd], axis=3).reshape(batch_size, 2 * rows_dev, 2 * cols_dev, outward)
    return (out + conv_bias).astype(jnp.bfloat16)


def per_device(fields, norm_gain, w_qkv, w_out, conv_weight, conv_bias):
    batch_size, rows_dev, cols_dev, width = fields.shape
    head_count = HEADS
    depth = width // head_count
    seq_count = batch_size * rows_dev
    half = cols_dev // 2
    from_left = shift(fields, "lon", 1, True)
    from_right = shift(fields, "lon", -1, True)
    opposite = jnp.concatenate(
        [
            shift(from_left[:, :, :half], "lon", 1, True),
            shift(from_right[:, :, half:], "lon", -1, True),
        ],
        axis=2,
    )
    w_q = w_qkv[:, :width].reshape(width, head_count, depth)
    w_k = w_qkv[:, width : 2 * width].reshape(width, head_count, depth)
    w_v = w_qkv[:, 2 * width :].reshape(width, head_count, depth)

    def keys_values(chunk):
        count = chunk.shape[2]
        normed = normalize(chunk, norm_gain).reshape(seq_count, count, width)
        kt = jnp.einsum("sld,dhe->shel", normed, w_k, preferred_element_type=jnp.float32)
        vt = jnp.einsum("sld,dhe->shel", normed, w_v, preferred_element_type=jnp.float32)
        shape = (seq_count * head_count, depth, count)
        return kt.astype(jnp.bfloat16).reshape(shape), vt.astype(jnp.bfloat16).reshape(shape)

    def queries(block):
        count = block.shape[2]
        normed = normalize(block, norm_gain).reshape(seq_count, count, width)
        qh = jnp.einsum("sld,dhe->shle", normed, w_q, preferred_element_type=jnp.float32)
        return qh.astype(jnp.bfloat16).reshape(seq_count * head_count, count, depth)

    pad = 16
    edge = jnp.concatenate(
        [from_left[:, :, -1:], from_right[:, :, :1], jnp.zeros_like(fields[:, :, : pad - 2])],
        axis=2,
    )
    qh = jnp.concatenate([queries(fields), queries(edge)], axis=1)
    local_kv = keys_values(fields)
    near_kv = keys_values(jnp.concatenate([from_left, from_right], axis=2))
    state = attend_chunk(qh, [near_kv[0]], [near_kv[1]])
    opposite_kv = keys_values(opposite)
    att, att_edge = attend_chunk(
        qh, [opposite_kv[0], local_kv[0]], [opposite_kv[1], local_kv[1]], state, last=pad
    )

    def finish(att, block, count):
        update = jnp.einsum(
            "shle,hef->slf",
            att.reshape(seq_count, head_count, count, depth),
            w_out.reshape(head_count, depth, width),
            preferred_element_type=jnp.float32,
        )
        update = update.reshape(batch_size, rows_dev, count, width)
        return (block.astype(jnp.float32) + update).astype(jnp.bfloat16)

    hidden = finish(att, fields, cols_dev)
    hidden_edge = finish(att_edge, edge, pad)
    ext = jnp.concatenate([hidden_edge[:, :, :1], hidden, hidden_edge[:, :, 1:2]], axis=2)
    return upsample(ext, conv_weight, conv_bias)


def solution(mesh):
    in_specs = (P(None, "lat", "lon", None), P(), P(), P(), P(), P())
    out_specs = P(None, "lat", "lon", None)
    return jax.shard_map(
        per_device, mesh=mesh, in_specs=in_specs, out_specs=out_specs, check_vma=False
    )
```
